512 devices in a mesh: grp: 8 (over y_hi, core), cp: 64 (over y_lo, x, z).
Axes of the slice: x: 4, y: 8 (y_hi: 4, y_lo: 2; y = y_hi * 2 + y_lo), z: 8, core: 2. Of those that a mesh axis runs over, the one named last changes fastest.
Arguments:
- query_long: bfloat16 [8, 32768, 1024], P('grp', 'cp'), may hold values from -20 to 20
- long_prompt_keys: bfloat16 [8, 32768, 512], P('grp', 'cp'), may hold values from -11 to 11
- long_prompt_values: bfloat16 [8, 32768, 512], P('grp', 'cp'), may hold values from -6 to 6
- long_length: int32 [8, 8], P('grp'), may hold values from 2048 to 4096, as said below
- short_prompt_queries: bfloat16 [8, 8192, 1024], P('grp', 'cp'), may hold values from -20 to 20
- short_prompt_keys: bfloat16 [8, 8192, 512], P('grp', 'cp'), may hold values from -11 to 11
- short_prompt_values: bfloat16 [8, 8192, 512], P('grp', 'cp'), may hold values from -6 to 6
- short_prompt_index: int32 [8, 64, 128], P('grp', 'cp'), may hold values from 0 to 3, never falling along the last dimension, each value on 1 to 64 neighbouring positions
- page_owner: int32 [8, 256], P('grp', 'cp'), may hold values from 0 to 7, as said below
- page_slot: int32 [8, 256], P('grp', 'cp'), may hold values from 0 to 3, as said below
Outputs:
- long_attention: bfloat16 [8, 32768, 1024], P('grp', 'cp')
- short_attention: bfloat16 [8, 8192, 1024], P('grp', 'cp')
- page_cache: bfloat16 [8, 256, 128, 1024], P('grp', 'cp')
The draws below stay inside these ranges and needn't reach their ends.
Inputs may be any that keep to these rules, and one draw needn't show every extreme that they name: `long_length`: each long prompt has from half of 4096 to 4096 tokens, and some prompt has exactly 4096. `page_owner`: page k of the device at grp index g and cp index c goes to grp index (g + an offset that depends on c and k) modulo the number of grp devices, at the same cp index. A device sends at most 1 of its pages to one owner, and exactly 1 to some owners. Every device receives exactly 4 pages. `page_slot`: the pages that reach one device take each of its slots once.
All inputs are finite; a program needn't handle non-finite values.
Results may differ from the reference program's by a relative error of at most 0.0055.
Values may be sent and summed in bfloat16 or wider, within the bound.
No kernel may reach another device: no remote copies, remote signals or barrier semaphores. Data moves between devices by JAX's collectives and lax.ppermute only.
A program may use at most 128 MiB of HBM per device.

```python
import math
import jax
import jax.numpy as jnp
import numpy as np
from jax import lax

QUERY_HEADS = 8
KEY_VALUE_HEADS = 4
HEAD_SIZE = 128
PAGE = 128
SPAN = 8
BLOCK_TOKENS = 256
SHORT_TOKENS = 128
SEGS = 4
LONG = 4096
LONG_PER_GROUP = 8
PAGES = 4
CAP = 1
SMOST = 64
N_GRP = 8
N_CP = 64


def long_pair(key):
    count_of_rows = N_CP * 2 * BLOCK_TOKENS
    key_query, random_key_keys = jax.random.split(key, 2)
    query_rows = 1.7 * jax.random.truncated_normal(key_query, -6.0, 6.0, (N_GRP, count_of_rows, QUERY_HEADS * HEAD_SIZE), jnp.float32)
    sampled_keys = 1.7 * jax.random.truncated_normal(random_key_keys, -6.0, 6.0, (N_GRP, count_of_rows, KEY_VALUE_HEADS * HEAD_SIZE), jnp.float32)
    return (query_rows, sampled_keys)


def short_pair(key):
    count_of_rows = N_CP * SHORT_TOKENS
    key_query, random_key_keys = jax.random.split(key, 2)
    query_rows = 1.7 * jax.random.truncated_normal(key_query, -6.0, 6.0, (N_GRP, count_of_rows, QUERY_HEADS * HEAD_SIZE), jnp.float32)
    sampled_keys = 1.7 * jax.random.truncated_normal(random_key_keys, -6.0, 6.0, (N_GRP, count_of_rows, KEY_VALUE_HEADS * HEAD_SIZE), jnp.float32)
    return (query_rows, sampled_keys)


def draw_query_long(key, part):
    return long_pair(jax.random.fold_in(key, 101))[0].astype(jnp.bfloat16)


def draw_long_prompt_keys(key, part):
    return long_pair(jax.random.fold_in(key, 101))[1].astype(jnp.bfloat16)


def draw_short_prompt_queries(key, part):
    return short_pair(jax.random.fold_in(key, 202))[0].astype(jnp.bfloat16)


def draw_short_prompt_keys(key, part):
    return short_pair(jax.random.fold_in(key, 202))[1].astype(jnp.bfloat16)


def draw_long_length(key, part):
    key_draw, key_pick = jax.random.split(jax.random.fold_in(key, 404))
    lengths = jax.random.randint(key_draw, (N_GRP * LONG_PER_GROUP,), LONG // 2, LONG + 1, dtype=jnp.int32)
    chosen = jax.random.randint(key_pick, (), 0, N_GRP * LONG_PER_GROUP, dtype=jnp.int32)
    lengths = jnp.where(jnp.arange(N_GRP * LONG_PER_GROUP, dtype=jnp.int32) == chosen, LONG, lengths)
    return lengths.reshape(N_GRP, LONG_PER_GROUP).astype(jnp.int32)


def page_table(key):
    key_pool, key_order, key_slots = jax.random.split(jax.random.fold_in(key, 303), 3)
    pool = jax.vmap(lambda sub_key: jax.random.permutation(sub_key, N_GRP))(jax.random.split(key_pool, N_CP))
    order = jax.vmap(lambda sub_key: jax.random.permutation(sub_key, PAGES))(jax.random.split(key_order, N_CP))
    offsets = jnp.take_along_axis(pool, order // CAP, axis=1)
    senders = jnp.arange(N_GRP, dtype=jnp.int32)[:, None, None]
    owners = (senders + offsets[None]) % N_GRP
    slot_perm = jax.vmap(lambda sub_key: jax.random.permutation(sub_key, PAGES))(jax.random.split(key_slots, N_CP * N_GRP)).reshape(N_CP, N_GRP, PAGES)
    column_ids = jnp.arange(N_CP, dtype=jnp.int32)[None, :, None]
    page_ids = jnp.arange(PAGES, dtype=jnp.int32)[None, None, :]
    slot_ids = slot_perm[column_ids, owners, page_ids]
    return (owners.reshape(N_GRP, N_CP * PAGES).astype(jnp.int32), slot_ids.reshape(N_GRP, N_CP * PAGES).astype(jnp.int32))


def draw_page_owner(key, part):
    return page_table(key)[0]


def draw_page_slot(key, part):
    return page_table(key)[1]


def levels(own_key, shape, cuts, least, top_value):
    loudness = 1.0
    for dim, shards_of in cuts:
        heights = jax.random.uniform(jax.random.fold_in(jax.random.fold_in(own_key, 6), dim), (shards_of,), jnp.float32, least / len(cuts), top_value / len(cuts))
        loudness = loudness * jnp.repeat(jnp.exp(heights), shape[dim] // shards_of).reshape((-1,) + (1,) * (len(shape) - 1 - dim))
    return loudness


def profile(number_of, total, limit, lean):
    weights = [(1 << 20) // math.isqrt(grade ** lean) + 1 for grade in range(2, number_of + 1)]
    spare, counts = total - limit - (number_of - 1), [1] * (number_of - 1)
    while spare > 0:
        free = [i for i in range(number_of - 1) if counts[i] < limit]
        mass, left = sum([weights[i] for i in free]), spare
        for i in free:
            more = min(limit - counts[i], max(1, left * weights[i] // mass), spare)
            counts[i] = counts[i] + more
            spare = spare - more
    return np.array([limit] + counts)


def ragged_sizes(own_key, amount, total, reach, slope):
    if amount == 2:
        one = jax.random.randint(own_key, (), max(1, total - reach), min(reach, total - 1) + 1)
        return jnp.stack([one, total - one])
    sizes = jnp.asarray(profile(amount, total, reach, slope), jnp.int32)
    pairs = (amount - 1) // 2
    source_of, sink = sizes[1:1 + 2 * pairs:2], sizes[2:2 + 2 * pairs:2]
    room = jnp.minimum(source_of - 1, reach - sink)
    passed = jax.random.randint(jax.random.fold_in(own_key, 1), (pairs,), 0, 1 << 20) % (room + 1)
    sizes = sizes.at[1:1 + 2 * pairs:2].set(source_of - passed).at[2:2 + 2 * pairs:2].set(sink + passed)
    return sizes[jax.random.permutation(jax.random.fold_in(own_key, 2), amount)]


def bell_draw(stream_key, shape, scale, limit, cuts=(), kind=jnp.bfloat16):
    loudness = levels(stream_key, shape, cuts, -0.22, 0.18) if cuts else 1.0
    entries = jax.random.normal(stream_key, shape, jnp.float32) * scale * loudness
    return jnp.minimum(jnp.maximum(entries, -limit), limit).astype(kind)


def setup_inputs(seed: int = 0) -> dict:
    seeds = jax.random.split(jax.random.key(seed), 11)
    query_long = draw_query_long(jax.random.fold_in(seeds[10], 71), 0)
    long_prompt_keys = draw_long_prompt_keys(jax.random.fold_in(seeds[10], 71), 0)
    long_prompt_values = bell_draw(seeds[2], (N_GRP, N_CP * 2 * BLOCK_TOKENS, KEY_VALUE_HEADS * HEAD_SIZE), 1.0, 6.0, ((0, 8), (1, 64)))
    long_length = draw_long_length(jax.random.fold_in(seeds[10], 71), 0)
    short_prompt_queries = draw_short_prompt_queries(jax.random.fold_in(seeds[10], 71), 0)
    short_prompt_keys = draw_short_prompt_keys(jax.random.fold_in(seeds[10], 71), 0)
    short_prompt_values = bell_draw(seeds[6], (N_GRP, N_CP * SHORT_TOKENS, KEY_VALUE_HEADS * HEAD_SIZE), 1.0, 6.0, ((0, 8), (1, 64)))
    short_prompt_index = jax.vmap(lambda own: jnp.searchsorted(jnp.cumsum(ragged_sizes(own, SEGS, SHORT_TOKENS, SMOST, 1)), jnp.arange(SHORT_TOKENS), side="right"))(jax.random.split(seeds[7], N_GRP * N_CP)).reshape((N_GRP, N_CP, SHORT_TOKENS)).astype(jnp.int32)
    page_owner = draw_page_owner(jax.random.fold_in(seeds[10], 71), 0)
    page_slot = draw_page_slot(jax.random.fold_in(seeds[10], 71), 0)
    return {"query_long": query_long, "long_prompt_keys": long_prompt_keys, "long_prompt_values": long_prompt_values, "long_length": long_length, "short_prompt_queries": short_prompt_queries, "short_prompt_keys": short_prompt_keys, "short_prompt_values": short_prompt_values, "short_prompt_index": short_prompt_index, "page_owner": page_owner, "page_slot": page_slot}


def long_positions():
    row_ids = jnp.arange(SPAN * 2 * BLOCK_TOKENS, dtype=jnp.int32)
    member = row_ids // (2 * BLOCK_TOKENS)
    second = row_ids // BLOCK_TOKENS % 2
    offset = row_ids % BLOCK_TOKENS
    block_ids = jnp.where(second == 0, member, 2 * SPAN - 1 - member)
    return block_ids * BLOCK_TOKENS + offset

def attend_rows(query_rows, key_row_block, value_row_block, visible):
    count_of_rows = query_rows.shape[0]
    grouped_heads = query_rows.astype(jnp.float32).reshape(count_of_rows, KEY_VALUE_HEADS, QUERY_HEADS // KEY_VALUE_HEADS, HEAD_SIZE)
    key_head_rows = key_row_block.astype(jnp.float32).reshape(key_row_block.shape[0], KEY_VALUE_HEADS, HEAD_SIZE)
    value_head_rows = value_row_block.astype(jnp.float32).reshape(value_row_block.shape[0], KEY_VALUE_HEADS, HEAD_SIZE)
    scores = jnp.einsum('rgjd,kgd->gjrk', grouped_heads, key_head_rows) / math.sqrt(HEAD_SIZE)
    scores = jnp.where(visible[None, None], scores, -jnp.inf)
    highest = lax.optimization_barrier(jnp.max(scores, axis=-1, keepdims=True))
    anchor = jnp.where(jnp.isfinite(highest), highest, 0.0)
    weights = jnp.where(visible[None, None], jnp.exp(scores - anchor), 0.0)
    weight_sum = lax.optimization_barrier(jnp.sum(weights, axis=-1))
    rounded = lax.optimization_barrier(weights.astype(jnp.bfloat16)).astype(jnp.float32)
    summed = jnp.einsum('gjrk,kgd->gjrd', rounded, value_head_rows)
    divisor = jnp.where(weight_sum > 0, weight_sum, 1.0)
    result = summed / divisor[..., None]
    return jnp.transpose(result, (2, 0, 1, 3)).reshape(count_of_rows, QUERY_HEADS * HEAD_SIZE)

def to_prompts(array_in):
    width = array_in.shape[-1]
    grouped = array_in.reshape(N_GRP, SPAN, LONG_PER_GROUP, 2 * BLOCK_TOKENS, width)
    grouped = jnp.transpose(grouped, (0, 2, 1, 3, 4))
    return grouped.reshape(N_GRP * LONG_PER_GROUP, SPAN * 2 * BLOCK_TOKENS, width)

def reference(query_long, long_prompt_keys, long_prompt_values, long_length, short_prompt_queries, short_prompt_keys, short_prompt_values, short_prompt_index, page_owner, page_slot):
    prompt_cycle_rows = SPAN * 2 * BLOCK_TOKENS
    positions = long_positions()
    step_rows = math.gcd(prompt_cycle_rows, 512)
    cycle_queries = to_prompts(query_long)
    prompt_cycle_keys = to_prompts(long_prompt_keys)
    prompt_cycle_values = to_prompts(long_prompt_values)
    cycle_lengths = long_length.reshape(N_GRP * LONG_PER_GROUP)

    def one_prompt(packed):
        query_rows, key_row_block, value_row_block, length = packed
        key_valid = positions < length

        def one_block(block_id):
            begin = block_id * step_rows
            query_part = lax.dynamic_slice_in_dim(query_rows, begin, step_rows, 0)
            query_pos = lax.dynamic_slice_in_dim(positions, begin, step_rows, 0)
            visible = (positions[None, :] <= query_pos[:, None]) & key_valid[None, :] & (query_pos[:, None] < length)
            return attend_rows(query_part, key_row_block, value_row_block, visible)
        blocks_out = lax.map(one_block, jnp.arange(prompt_cycle_rows // step_rows, dtype=jnp.int32))
        return blocks_out.reshape(prompt_cycle_rows, QUERY_HEADS * HEAD_SIZE)
    long_out = lax.map(one_prompt, (cycle_queries, prompt_cycle_keys, prompt_cycle_values, cycle_lengths))
    long_out = long_out.reshape(N_GRP, LONG_PER_GROUP, SPAN, 2 * BLOCK_TOKENS, QUERY_HEADS * HEAD_SIZE)
    long_out = jnp.transpose(long_out, (0, 2, 1, 3, 4))
    long_attention = long_out.reshape(N_GRP, N_CP * 2 * BLOCK_TOKENS, QUERY_HEADS * HEAD_SIZE).astype(jnp.bfloat16)
    order_ids = jnp.arange(SHORT_TOKENS, dtype=jnp.int32)
    causal = order_ids[None, :] <= order_ids[:, None]

    def single_device(packed):
        query_rows, key_row_block, value_row_block, segment_row = packed
        visible = causal & (segment_row[None, :] == segment_row[:, None])
        return attend_rows(query_rows, key_row_block, value_row_block, visible)
    short_prompt_output = lax.map(single_device, (short_prompt_queries.reshape(N_GRP * N_CP, SHORT_TOKENS, QUERY_HEADS * HEAD_SIZE), short_prompt_keys.reshape(N_GRP * N_CP, SHORT_TOKENS, KEY_VALUE_HEADS * HEAD_SIZE), short_prompt_values.reshape(N_GRP * N_CP, SHORT_TOKENS, KEY_VALUE_HEADS * HEAD_SIZE), short_prompt_index.reshape(N_GRP * N_CP, SHORT_TOKENS)))
    short_attention = short_prompt_output.reshape(N_GRP, N_CP * SHORT_TOKENS, QUERY_HEADS * HEAD_SIZE).astype(jnp.bfloat16)
    column_width = 2 * KEY_VALUE_HEADS * HEAD_SIZE
    joined = jnp.concatenate([long_prompt_keys, long_prompt_values], axis=-1).reshape(N_GRP, N_CP, PAGES, PAGE, column_width)
    page_pos = jnp.repeat(positions.reshape(SPAN, PAGES, PAGE), LONG_PER_GROUP, axis=0)
    device_lengths = jnp.tile(long_length, (1, SPAN))
    valid = page_pos[None] < device_lengths[:, :, None, None]
    content = jnp.where(valid[..., None], joined, jnp.zeros_like(joined))
    owners = page_owner.reshape(N_GRP, N_CP, PAGES)
    slot_ids = page_slot.reshape(N_GRP, N_CP, PAGES)
    columns = jnp.broadcast_to(jnp.arange(N_CP, dtype=jnp.int32)[None, :, None], owners.shape)
    cache = jnp.zeros((N_GRP, N_CP, PAGES, PAGE, column_width), jnp.bfloat16)
    cache = cache.at[owners, columns, slot_ids].set(content)
    page_cache = cache.reshape(N_GRP, N_CP * PAGES, PAGE, column_width)
    return (long_attention, short_attention, page_cache)
```

```python
import math

import jax
import jax.numpy as jnp
from jax import lax
from jax.experimental import pallas as pl
from jax.experimental.pallas import tpu as pltpu
from jax.sharding import Mesh
from jax.sharding import PartitionSpec as P

QUERY_HEADS = 8
KEY_VALUE_HEADS = 4
HEAD_SIZE = 128
PAGE = 128
SPAN = 8


def head_scores(query_rows, key_row_block, visible):
    paired_count, count_of_rows = (query_rows.shape[0], query_rows.shape[1])
    grouped_heads = query_rows.reshape(
        paired_count, count_of_rows, KEY_VALUE_HEADS, QUERY_HEADS // KEY_VALUE_HEADS, HEAD_SIZE
    )
    key_head_rows = key_row_block.reshape(
        paired_count, key_row_block.shape[1], KEY_VALUE_HEADS, HEAD_SIZE
    )
    scores = jnp.einsum(
        "prgjd,pkgd->pgjrk", grouped_heads, key_head_rows, preferred_element_type=jnp.float32
    )
    scores = scores / math.sqrt(HEAD_SIZE)
    return jnp.where(visible[:, None, None], scores, -jnp.inf)


def block_stats(query_rows, key_row_block, value_row_block, visible):
    scores = head_scores(query_rows, key_row_block, visible)
    highest = jnp.max(scores, axis=-1)
    anchor = jnp.where(jnp.isfinite(highest), highest, 0.0)
    weights = jnp.where(visible[:, None, None], jnp.exp(scores - anchor[..., None]), 0.0)
    weight_sum = jnp.sum(weights, axis=-1)
    value_head_rows = value_row_block.reshape(
        value_row_block.shape[0], value_row_block.shape[1], KEY_VALUE_HEADS, HEAD_SIZE
    )
    summed = jnp.einsum(
        "pgjrk,pkgd->pgjrd",
        weights.astype(jnp.bfloat16),
        value_head_rows,
        preferred_element_type=jnp.float32,
    )
    return (highest, weight_sum, summed)


def take_pair(pair_stats, position_in):
    return jax.tree.map(lambda leaf_array: leaf_array[position_in], pair_stats)


def finish_rows(stats_in, live_rows):
    highest, weight_sum, summed = stats_in
    divisor = jnp.where(weight_sum > 0, weight_sum, 1.0)
    result = summed / divisor[..., None]
    result = jnp.where(live_rows[None, None, :, None], result, 0.0)
    return jnp.transpose(result, (2, 0, 1, 3)).reshape(live_rows.shape[0], QUERY_HEADS * HEAD_SIZE)


def flash_kernel(info_ref, q_ref, k_ref, v_ref, o_ref, m_sc, l_sc, acc_sc, *, block, blocks):
    qb = pl.program_id(0)
    kc = pl.program_id(1)
    member = info_ref[0]
    length = info_ref[1]
    bq = jnp.where(qb == 0, member, 2 * SPAN - 1 - member)
    kmax = jnp.minimum(bq, (length - 1) // block)

    @pl.when(kc == 0)
    def _init():
        m_sc[...] = jnp.full(m_sc.shape, -jnp.inf, jnp.float32)
        l_sc[...] = jnp.zeros(l_sc.shape, jnp.float32)
        acc_sc[...] = jnp.zeros(acc_sc.shape, jnp.float32)

    @pl.when(kc <= kmax)
    def _step():
        q_pos = bq * block + lax.broadcasted_iota(jnp.int32, (block, block), 0)
        k_pos = kc * block + lax.broadcasted_iota(jnp.int32, (block, block), 1)
        visible = (k_pos <= q_pos) & (k_pos < length) & (q_pos < length)
        scale = 1.0 / math.sqrt(HEAD_SIZE)
        for g in range(KEY_VALUE_HEADS):
            k = k_ref[0, :, g * HEAD_SIZE:(g + 1) * HEAD_SIZE]
            v = v_ref[0, :, g * HEAD_SIZE:(g + 1) * HEAD_SIZE]
            for jj in range(QUERY_HEADS // KEY_VALUE_HEADS):
                h = g * (QUERY_HEADS // KEY_VALUE_HEADS) + jj
                q = q_ref[:, h * HEAD_SIZE:(h + 1) * HEAD_SIZE]
                s = lax.dot_general(
                    q, k, (((1,), (1,)), ((), ())), preferred_element_type=jnp.float32
                ) * scale
                s = jnp.where(visible, s, -jnp.inf)
                m_old = m_sc[h]
                m_new = jnp.maximum(m_old, jnp.max(s, axis=-1, keepdims=True))
                anchor = jnp.where(m_new > -jnp.inf, m_new, 0.0)
                p = jnp.where(visible, jnp.exp(s - anchor), 0.0)
                alpha = jnp.exp(m_old - anchor)
                l_sc[h] = alpha * l_sc[h] + jnp.sum(p, axis=-1, keepdims=True)
                acc_sc[h] = alpha * acc_sc[h] + jnp.dot(
                    p.astype(jnp.bfloat16), v, preferred_element_type=jnp.float32
                )
                m_sc[h] = m_new

    @pl.when(kc == blocks - 1)
    def _finish():
        for h in range(QUERY_HEADS):
            l = l_sc[h]
            divisor = jnp.where(l > 0, l, 1.0)
            o_ref[:, h * HEAD_SIZE:(h + 1) * HEAD_SIZE] = (acc_sc[h] / divisor).astype(o_ref.dtype)


def long_attention(info, query_rows, kv_all, block):
    blocks = 2 * SPAN
    half_kv = kv_all.shape[-1] // 2

    def kv_index(qb, kc, info_ref, which):
        member = info_ref[0]
        length = info_ref[1]
        bq = jnp.where(qb == 0, member, 2 * SPAN - 1 - member)
        kk = jnp.minimum(kc, jnp.minimum(bq, (length - 1) // block))
        j = jnp.where(kk < SPAN, 2 * kk, 2 * (2 * SPAN - 1 - kk) + 1)
        return (j, 0, which)

    grid_spec = pltpu.PrefetchScalarGridSpec(
        num_scalar_prefetch=1,
        grid=(2, blocks),
        in_specs=[
            pl.BlockSpec((block, query_rows.shape[1]), lambda qb, kc, info_ref: (qb, 0)),
            pl.BlockSpec((1, block, half_kv), lambda qb, kc, info_ref: kv_index(qb, kc, info_ref, 0)),
            pl.BlockSpec((1, block, half_kv), lambda qb, kc, info_ref: kv_index(qb, kc, info_ref, 1)),
        ],
        out_specs=pl.BlockSpec((block, query_rows.shape[1]), lambda qb, kc, info_ref: (qb, 0)),
        scratch_shapes=[
            pltpu.VMEM((QUERY_HEADS, block, 1), jnp.float32),
            pltpu.VMEM((QUERY_HEADS, block, 1), jnp.float32),
            pltpu.VMEM((QUERY_HEADS, block, HEAD_SIZE), jnp.float32),
        ],
    )
    flops = 4 * 17 * block * block * HEAD_SIZE * QUERY_HEADS
    return pl.pallas_call(
        lambda *refs: flash_kernel(*refs, block=block, blocks=blocks),
        grid_spec=grid_spec,
        out_shape=jax.ShapeDtypeStruct(query_rows.shape, jnp.bfloat16),
        compiler_params=pltpu.CompilerParams(
            dimension_semantics=("arbitrary", "arbitrary"),
        ),
        cost_estimate=pl.CostEstimate(
            flops=flops,
            transcendentals=17 * block * block * QUERY_HEADS,
            bytes_accessed=2 * query_rows.size * 2 + 17 * block * kv_all.shape[-1] * 2,
        ),
        name="long_flash",
    )(info, query_rows, kv_all, kv_all)


def per_device(
    query_long,
    long_prompt_keys,
    long_prompt_values,
    long_length,
    short_prompt_queries,
    short_prompt_keys,
    short_prompt_values,
    short_prompt_index,
    page_owner,
    page_slot,
):
    half_rows = query_long.shape[1] // 2
    member = lax.axis_index("m")
    group_id = lax.axis_index("r")
    length = lax.dynamic_index_in_dim(long_length[0], group_id, 0, keepdims=False)
    offsets = jnp.arange(half_rows, dtype=jnp.int32)
    pos_first = member * half_rows + offsets
    pos_second = (2 * SPAN - 1 - member) * half_rows + offsets

    key_row_block = long_prompt_keys[0]
    value_row_block = long_prompt_values[0]
    kv_rows = jnp.concatenate([key_row_block, value_row_block], axis=-1)

    kv_all = lax.all_gather(kv_rows, "m", axis=0, tiled=False)
    kv_all = kv_all.reshape(2 * SPAN, half_rows, kv_rows.shape[-1])
    info = jnp.stack([member, length]).astype(jnp.int32)
    long_out = long_attention(info, query_long[0], kv_all, half_rows)

    segment_row = short_prompt_index[0, 0]
    order_ids = jnp.arange(segment_row.shape[0], dtype=jnp.int32)
    short_visible = (order_ids[None, :] <= order_ids[:, None]) & (
        segment_row[None, :] == segment_row[:, None]
    )
    short_stats = block_stats(
        short_prompt_queries[0][None],
        short_prompt_keys[0][None],
        short_prompt_values[0][None],
        short_visible[None],
    )
    short_prompt_output = finish_rows(take_pair(short_stats, 0), order_ids >= 0)

    row_positions = jnp.concatenate([pos_first, pos_second])
    kv_rows = jnp.where((row_positions < length)[:, None], kv_rows, jnp.zeros_like(kv_rows))
    page_count = kv_rows.shape[0] // PAGE
    page_width = kv_rows.shape[1]
    page_data = kv_rows.reshape(page_count, PAGE * page_width)
    owners = page_owner[0]
    slot_ids = page_slot[0]
    groups = lax.axis_size("grp")
    capacity = max(1, page_count // groups)
    page_ids = jnp.arange(page_count, dtype=jnp.int32)
    earlier = jnp.sum(
        (owners[None, :] == owners[:, None]) & (page_ids[None, :] < page_ids[:, None]), axis=1
    )
    target = owners * capacity + earlier
    bucket_ids = jnp.arange(groups * capacity, dtype=jnp.int32)
    onehot = target[None, :] == bucket_ids[:, None]
    outgoing = jnp.dot(
        onehot.astype(jnp.bfloat16), page_data, preferred_element_type=jnp.float32
    ).astype(jnp.bfloat16)
    out_slots = jnp.max(jnp.where(onehot, slot_ids[None, :], -1), axis=1)
    incoming, in_slots = (
        lax.all_to_all(
            outgoing.reshape(groups, capacity, PAGE * page_width),
            "grp",
            split_axis=0,
            concat_axis=0,
            tiled=True,
        ),
        lax.all_to_all(
            out_slots.reshape(groups, capacity), "grp", split_axis=0, concat_axis=0, tiled=True
        ),
    )
    chooser = in_slots.reshape(-1)[None, :] == page_ids[:, None]
    stored = jnp.dot(
        chooser.astype(jnp.bfloat16),
        incoming.reshape(groups * capacity, PAGE * page_width),
        preferred_element_type=jnp.float32,
    ).astype(jnp.bfloat16)
    return (
        long_out[None],
        short_prompt_output[None].astype(jnp.bfloat16),
        stored.reshape(1, page_count, PAGE, page_width),
    )


def solution(mesh):
    n_grp = mesh.shape["grp"]
    n_cp = mesh.shape["cp"]
    stride = n_cp // SPAN
    split_mesh = Mesh(mesh.devices.reshape(n_grp, SPAN, stride), ("grp", "m", "r"))
    rows = ("m", "r")
    in_specs = (
        P("grp", rows, None),
        P("grp", rows, None),
        P("grp", rows, None),
        P("grp", None),
        P("grp", rows, None),
        P("grp", rows, None),
        P("grp", rows, None),
        P("grp", rows, None),
        P("grp", rows),
        P("grp", rows),
    )
    out_specs = (P("grp", rows, None), P("grp", rows, None), P("grp", rows, None, None))
    return jax.shard_map(
        per_device, mesh=split_mesh, in_specs=in_specs, out_specs=out_specs, check_vma=False
    )
```

```python
import math

import jax
import jax.numpy as jnp
from jax import lax
from jax.experimental import pallas as pl
from jax.experimental.pallas import tpu as pltpu
from jax.sharding import Mesh
from jax.sharding import PartitionSpec as P

QUERY_HEADS = 8
KEY_VALUE_HEADS = 4
HEAD_SIZE = 128
PAGE = 128
SPAN = 8


def head_scores(query_rows, key_row_block, visible):
    paired_count, count_of_rows = (query_rows.shape[0], query_rows.shape[1])
    grouped_heads = query_rows.reshape(
        paired_count, count_of_rows, KEY_VALUE_HEADS, QUERY_HEADS // KEY_VALUE_HEADS, HEAD_SIZE
    )
    key_head_rows = key_row_block.reshape(
        paired_count, key_row_block.shape[1], KEY_VALUE_HEADS, HEAD_SIZE
    )
    scores = jnp.einsum(
        "prgjd,pkgd->pgjrk", grouped_heads, key_head_rows, preferred_element_type=jnp.float32
    )
    scores = scores / math.sqrt(HEAD_SIZE)
    return jnp.where(visible[:, None, None], scores, -jnp.inf)


def block_stats(query_rows, key_row_block, value_row_block, visible):
    scores = head_scores(query_rows, key_row_block, visible)
    highest = jnp.max(scores, axis=-1)
    anchor = jnp.where(jnp.isfinite(highest), highest, 0.0)
    weights = jnp.where(visible[:, None, None], jnp.exp(scores - anchor[..., None]), 0.0)
    weight_sum = jnp.sum(weights, axis=-1)
    value_head_rows = value_row_block.reshape(
        value_row_block.shape[0], value_row_block.shape[1], KEY_VALUE_HEADS, HEAD_SIZE
    )
    summed = jnp.einsum(
        "pgjrk,pkgd->pgjrd",
        weights.astype(jnp.bfloat16),
        value_head_rows,
        preferred_element_type=jnp.float32,
    )
    return (highest, weight_sum, summed)


def take_pair(pair_stats, position_in):
    return jax.tree.map(lambda leaf_array: leaf_array[position_in], pair_stats)


def finish_rows(stats_in, live_rows):
    highest, weight_sum, summed = stats_in
    divisor = jnp.where(weight_sum > 0, weight_sum, 1.0)
    result = summed / divisor[..., None]
    result = jnp.where(live_rows[None, None, :, None], result, 0.0)
    return jnp.transpose(result, (2, 0, 1, 3)).reshape(live_rows.shape[0], QUERY_HEADS * HEAD_SIZE)


def flash_kernel(info_ref, q_ref, k_ref, v_ref, o_ref, m_sc, l_sc, acc_sc, *, block):
    step = pl.program_id(0)
    member = info_ref[0]
    length = info_ref[1]
    later = step > member
    bq = jnp.where(later, 2 * SPAN - 1 - member, member)
    kc = jnp.where(later, step - member - 1, step)
    kmax = jnp.minimum(bq, (length - 1) // block)
    scale = 1.0 / math.sqrt(HEAD_SIZE)

    @pl.when(kc == 0)
    def _init():
        m_sc[...] = jnp.full(m_sc.shape, -jnp.inf, jnp.float32)
        l_sc[...] = jnp.zeros(l_sc.shape, jnp.float32)
        acc_sc[...] = jnp.zeros(acc_sc.shape, jnp.float32)

    def attend(visible):
        for g in range(KEY_VALUE_HEADS):
            k = k_ref[0, :, g * HEAD_SIZE:(g + 1) * HEAD_SIZE]
            v = v_ref[0, :, g * HEAD_SIZE:(g + 1) * HEAD_SIZE]
            for jj in range(QUERY_HEADS // KEY_VALUE_HEADS):
                h = g * (QUERY_HEADS // KEY_VALUE_HEADS) + jj
                q = q_ref[:, h * HEAD_SIZE:(h + 1) * HEAD_SIZE]
                s = lax.dot_general(
                    q, k, (((1,), (1,)), ((), ())), preferred_element_type=jnp.float32
                ) * scale
                if visible is not None:
                    s = jnp.where(visible, s, -jnp.inf)
                m_old = m_sc[h]
                m_new = jnp.maximum(m_old, jnp.max(s, axis=-1, keepdims=True))
                if visible is not None:
                    anchor = jnp.where(m_new > -jnp.inf, m_new, 0.0)
                    p = jnp.where(visible, jnp.exp(s - anchor), 0.0)
                else:
                    anchor = m_new
                    p = jnp.exp(s - anchor)
                alpha = jnp.exp(m_old - anchor)
                l_sc[h] = alpha * l_sc[h] + jnp.sum(p, axis=-1, keepdims=True)
                acc_sc[h] = alpha * acc_sc[h] + jnp.dot(
                    p.astype(jnp.bfloat16), v, preferred_element_type=jnp.float32
                )
                m_sc[h] = m_new

    edge = (kc == bq) | ((kc + 1) * block > length)

    @pl.when((kc <= kmax) & edge)
    def _edge_step():
        q_pos = bq * block + lax.broadcasted_iota(jnp.int32, (block, block), 0)
        k_pos = kc * block + lax.broadcasted_iota(jnp.int32, (block, block), 1)
        attend((k_pos <= q_pos) & (k_pos < length))

    @pl.when((kc <= kmax) & jnp.logical_not(edge))
    def _full_step():
        attend(None)

    @pl.when(kc == bq)
    def _finish():
        live = (bq * block + lax.broadcasted_iota(jnp.int32, (block, 1), 0)) < length
        for h in range(QUERY_HEADS):
            l = l_sc[h]
            divisor = jnp.where(l > 0, l, 1.0)
            result = jnp.where(live, acc_sc[h] / divisor, 0.0)
            o_ref[:, h * HEAD_SIZE:(h + 1) * HEAD_SIZE] = result.astype(o_ref.dtype)


def long_attention(info, query_rows, kv_all, block):
    steps = 2 * SPAN + 1
    half_kv = kv_all.shape[-1] // 2
    x_size = SPAN // 2

    def q_index(step, info_ref):
        return (jnp.where(step > info_ref[0], 1, 0), 0)

    def kv_index(step, info_ref, which):
        member = info_ref[0]
        length = info_ref[1]
        later = step > member
        bq = jnp.where(later, 2 * SPAN - 1 - member, member)
        kc = jnp.where(later, step - member - 1, step)
        kk = jnp.minimum(kc, jnp.minimum(bq, (length - 1) // block))
        source = jnp.where(kk < SPAN, kk, 2 * SPAN - 1 - kk)
        half = jnp.where(kk < SPAN, 0, 1)
        j = (source % x_size) * 4 + (source // x_size) * 2 + half
        return (j, 0, which)

    grid_spec = pltpu.PrefetchScalarGridSpec(
        num_scalar_prefetch=1,
        grid=(steps,),
        in_specs=[
            pl.BlockSpec((block, query_rows.shape[1]), q_index),
            pl.BlockSpec((1, block, half_kv), lambda step, info_ref: kv_index(step, info_ref, 0)),
            pl.BlockSpec((1, block, half_kv), lambda step, info_ref: kv_index(step, info_ref, 1)),
        ],
        out_specs=pl.BlockSpec((block, query_rows.shape[1]), q_index),
        scratch_shapes=[
            pltpu.VMEM((QUERY_HEADS, block, 1), jnp.float32),
            pltpu.VMEM((QUERY_HEADS, block, 1), jnp.float32),
            pltpu.VMEM((QUERY_HEADS, block, HEAD_SIZE), jnp.float32),
        ],
    )
    flops = 4 * steps * block * block * HEAD_SIZE * QUERY_HEADS
    return pl.pallas_call(
        lambda *refs: flash_kernel(*refs, block=block),
        grid_spec=grid_spec,
        out_shape=jax.ShapeDtypeStruct(query_rows.shape, jnp.bfloat16),
        compiler_params=pltpu.CompilerParams(dimension_semantics=("arbitrary",)),
        cost_estimate=pl.CostEstimate(
            flops=flops,
            transcendentals=steps * block * block * QUERY_HEADS,
            bytes_accessed=2 * query_rows.size * 2 + steps * block * kv_all.shape[-1] * 2,
        ),
        name="long_flash",
    )(info, query_rows, kv_all, kv_all)


def per_device(
    query_long,
    long_prompt_keys,
    long_prompt_values,
    long_length,
    short_prompt_queries,
    short_prompt_keys,
    short_prompt_values,
    short_prompt_index,
    page_owner,
    page_slot,
):
    half_rows = query_long.shape[1] // 2
    member = lax.axis_index("yl") * lax.axis_size("xx") + lax.axis_index("xx")
    group_id = lax.axis_index("r")
    length = lax.dynamic_index_in_dim(long_length[0], group_id, 0, keepdims=False)
    offsets = jnp.arange(half_rows, dtype=jnp.int32)
    pos_first = member * half_rows + offsets
    pos_second = (2 * SPAN - 1 - member) * half_rows + offsets

    key_row_block = long_prompt_keys[0]
    value_row_block = long_prompt_values[0]
    kv_rows = jnp.concatenate([key_row_block, value_row_block], axis=-1)

    kv_pair = lax.all_gather(kv_rows, "yl", axis=0, tiled=False)
    kv_all = lax.all_gather(kv_pair, "xx", axis=0, tiled=False)
    kv_all = kv_all.reshape(2 * SPAN, half_rows, kv_rows.shape[-1])
    info = jnp.stack([member, length]).astype(jnp.int32)
    long_out = long_attention(info, query_long[0], kv_all, half_rows)

    segment_row = short_prompt_index[0, 0]
    order_ids = jnp.arange(segment_row.shape[0], dtype=jnp.int32)
    short_visible = (order_ids[None, :] <= order_ids[:, None]) & (
        segment_row[None, :] == segment_row[:, None]
    )
    short_stats = block_stats(
        short_prompt_queries[0][None],
        short_prompt_keys[0][None],
        short_prompt_values[0][None],
        short_visible[None],
    )
    short_prompt_output = finish_rows(take_pair(short_stats, 0), order_ids >= 0)

    row_positions = jnp.concatenate([pos_first, pos_second])
    kv_rows = jnp.where((row_positions < length)[:, None], kv_rows, jnp.zeros_like(kv_rows))
    page_count = kv_rows.shape[0] // PAGE
    page_width = kv_rows.shape[1]
    page_data = kv_rows.reshape(page_count, PAGE * page_width)
    owners = page_owner[0]
    slot_ids = page_slot[0]
    groups = lax.axis_size("grp")
    capacity = max(1, page_count // groups)
    page_ids = jnp.arange(page_count, dtype=jnp.int32)
    earlier = jnp.sum(
        (owners[None, :] == owners[:, None]) & (page_ids[None, :] < page_ids[:, None]), axis=1
    )
    target = owners * capacity + earlier
    bucket_ids = jnp.arange(groups * capacity, dtype=jnp.int32)
    onehot = target[None, :] == bucket_ids[:, None]
    outgoing = jnp.dot(
        onehot.astype(jnp.bfloat16), page_data, preferred_element_type=jnp.float32
    ).astype(jnp.bfloat16)
    out_slots = jnp.max(jnp.where(onehot, slot_ids[None, :], -1), axis=1)
    incoming, in_slots = (
        lax.all_to_all(
            outgoing.reshape(groups, capacity, PAGE * page_width),
            "grp",
            split_axis=0,
            concat_axis=0,
            tiled=True,
        ),
        lax.all_to_all(
            out_slots.reshape(groups, capacity), "grp", split_axis=0, concat_axis=0, tiled=True
        ),
    )
    chooser = in_slots.reshape(-1)[None, :] == page_ids[:, None]
    stored = jnp.dot(
        chooser.astype(jnp.bfloat16),
        incoming.reshape(groups * capacity, PAGE * page_width),
        preferred_element_type=jnp.float32,
    ).astype(jnp.bfloat16)
    return (
        long_out[None],
        short_prompt_output[None].astype(jnp.bfloat16),
        stored.reshape(1, page_count, PAGE, page_width),
    )


def solution(mesh):
    n_grp = mesh.shape["grp"]
    n_cp = mesh.shape["cp"]
    stride = n_cp // SPAN
    split_mesh = Mesh(
        mesh.devices.reshape(n_grp, 2, SPAN // 2, stride), ("grp", "yl", "xx", "r")
    )
    rows = ("yl", "xx", "r")
    in_specs = (
        P("grp", rows, None),
        P("grp", rows, None),
        P("grp", rows, None),
        P("grp", None),
        P("grp", rows, None),
        P("grp", rows, None),
        P("grp", rows, None),
        P("grp", rows, None),
        P("grp", rows),
        P("grp", rows),
    )
    out_specs = (P("grp", rows, None), P("grp", rows, None), P("grp", rows, None, None))
    return jax.shard_map(
        per_device, mesh=split_mesh, in_specs=in_specs, out_specs=out_specs, check_vma=False
    )
```

```python
import math

import jax
import jax.numpy as jnp
from jax import lax
from jax.experimental import pallas as pl
from jax.experimental.pallas import tpu as pltpu
from jax.sharding import Mesh
from jax.sharding import PartitionSpec as P

QUERY_HEADS = 8
KEY_VALUE_HEADS = 4
HEAD_SIZE = 128
PAGE = 128
SPAN = 8


def head_scores(query_rows, key_row_block, visible):
    paired_count, count_of_rows = (query_rows.shape[0], query_rows.shape[1])
    grouped_heads = query_rows.reshape(
        paired_count, count_of_rows, KEY_VALUE_HEADS, QUERY_HEADS // KEY_VALUE_HEADS, HEAD_SIZE
    )
    key_head_rows = key_row_block.reshape(
        paired_count, key_row_block.shape[1], KEY_VALUE_HEADS, HEAD_SIZE
    )
    scores = jnp.einsum(
        "prgjd,pkgd->pgjrk", grouped_heads, key_head_rows, preferred_element_type=jnp.float32
    )
    scores = scores / math.sqrt(HEAD_SIZE)
    return jnp.where(visible[:, None, None], scores, -jnp.inf)


def block_stats(query_rows, key_row_block, value_row_block, visible):
    scores = head_scores(query_rows, key_row_block, visible)
    highest = jnp.max(scores, axis=-1)
    anchor = jnp.where(jnp.isfinite(highest), highest, 0.0)
    weights = jnp.where(visible[:, None, None], jnp.exp(scores - anchor[..., None]), 0.0)
    weight_sum = jnp.sum(weights, axis=-1)
    value_head_rows = value_row_block.reshape(
        value_row_block.shape[0], value_row_block.shape[1], KEY_VALUE_HEADS, HEAD_SIZE
    )
    summed = jnp.einsum(
        "pgjrk,pkgd->pgjrd",
        weights.astype(jnp.bfloat16),
        value_head_rows,
        preferred_element_type=jnp.float32,
    )
    return (highest, weight_sum, summed)


def take_pair(pair_stats, position_in):
    return jax.tree.map(lambda leaf_array: leaf_array[position_in], pair_stats)


def finish_rows(stats_in, live_rows):
    highest, weight_sum, summed = stats_in
    divisor = jnp.where(weight_sum > 0, weight_sum, 1.0)
    result = summed / divisor[..., None]
    result = jnp.where(live_rows[None, None, :, None], result, 0.0)
    return jnp.transpose(result, (2, 0, 1, 3)).reshape(live_rows.shape[0], QUERY_HEADS * HEAD_SIZE)


def flash_kernel(info_ref, q_ref, k_ref, v_ref, o_ref, m_sc, l_sc, acc_sc, *, block):
    step = pl.program_id(0)
    member = info_ref[0]
    length = info_ref[1]
    later = step > member
    bq = jnp.where(later, 2 * SPAN - 1 - member, member)
    kc = jnp.where(later, step - member - 1, step)
    kmax = jnp.minimum(bq, (length - 1) // block)
    scale = 1.0 / math.sqrt(HEAD_SIZE)

    @pl.when(kc == 0)
    def _init():
        m_sc[...] = jnp.full(m_sc.shape, -jnp.inf, jnp.float32)
        l_sc[...] = jnp.zeros(l_sc.shape, jnp.float32)
        acc_sc[...] = jnp.zeros(acc_sc.shape, jnp.float32)

    def attend(visible):
        for g in range(KEY_VALUE_HEADS):
            k = k_ref[0, :, g * HEAD_SIZE:(g + 1) * HEAD_SIZE]
            v = v_ref[0, :, g * HEAD_SIZE:(g + 1) * HEAD_SIZE]
            for jj in range(QUERY_HEADS // KEY_VALUE_HEADS):
                h = g * (QUERY_HEADS // KEY_VALUE_HEADS) + jj
                q = q_ref[:, h * HEAD_SIZE:(h + 1) * HEAD_SIZE]
                s = lax.dot_general(
                    q, k, (((1,), (1,)), ((), ())), preferred_element_type=jnp.float32
                ) * scale
                if visible is not None:
                    s = jnp.where(visible, s, -jnp.inf)
                m_old = m_sc[h]
                m_new = jnp.maximum(m_old, jnp.max(s, axis=-1, keepdims=True))
                if visible is not None:
                    anchor = jnp.where(m_new > -jnp.inf, m_new, 0.0)
                    p = jnp.where(visible, jnp.exp(s - anchor), 0.0)
                else:
                    anchor = m_new
                    p = jnp.exp(s - anchor)
                alpha = jnp.exp(m_old - anchor)
                l_sc[h] = alpha * l_sc[h] + jnp.sum(p, axis=-1, keepdims=True)
                acc_sc[h] = alpha * acc_sc[h] + jnp.dot(
                    p.astype(jnp.bfloat16), v, preferred_element_type=jnp.float32
                )
                m_sc[h] = m_new

    edge = (kc == bq) | ((kc + 1) * block > length)

    @pl.when((kc <= kmax) & edge)
    def _edge_step():
        q_pos = bq * block + lax.broadcasted_iota(jnp.int32, (block, block), 0)
        k_pos = kc * block + lax.broadcasted_iota(jnp.int32, (block, block), 1)
        attend((k_pos <= q_pos) & (k_pos < length))

    @pl.when((kc <= kmax) & jnp.logical_not(edge))
    def _full_step():
        attend(None)

    @pl.when(kc == bq)
    def _finish():
        live = (bq * block + lax.broadcasted_iota(jnp.int32, (block, 1), 0)) < length
        for h in range(QUERY_HEADS):
            l = l_sc[h]
            divisor = jnp.where(l > 0, l, 1.0)
            result = jnp.where(live, acc_sc[h] / divisor, 0.0)
            o_ref[:, h * HEAD_SIZE:(h + 1) * HEAD_SIZE] = result.astype(o_ref.dtype)


def long_attention(info, query_rows, kv_all, block):
    steps = 2 * SPAN + 1
    half_kv = kv_all.shape[-1] // 2
    x_size = SPAN // 2

    def q_index(step, info_ref):
        return (jnp.where(step > info_ref[0], 1, 0), 0)

    def kv_index(step, info_ref, which):
        member = info_ref[0]
        length = info_ref[1]
        later = step > member
        bq = jnp.where(later, 2 * SPAN - 1 - member, member)
        kc = jnp.where(later, step - member - 1, step)
        kk = jnp.minimum(kc, jnp.minimum(bq, (length - 1) // block))
        source = jnp.where(kk < SPAN, kk, 2 * SPAN - 1 - kk)
        half = jnp.where(kk < SPAN, 0, 1)
        dy = (member // x_size - source // x_size + 2) % 2
        dx = (member % x_size - source % x_size + x_size) % x_size
        j = (dy * x_size + dx) * 2 + half
        return (j, 0, which)

    grid_spec = pltpu.PrefetchScalarGridSpec(
        num_scalar_prefetch=1,
        grid=(steps,),
        in_specs=[
            pl.BlockSpec((block, query_rows.shape[1]), q_index),
            pl.BlockSpec((1, block, half_kv), lambda step, info_ref: kv_index(step, info_ref, 0)),
            pl.BlockSpec((1, block, half_kv), lambda step, info_ref: kv_index(step, info_ref, 1)),
        ],
        out_specs=pl.BlockSpec((block, query_rows.shape[1]), q_index),
        scratch_shapes=[
            pltpu.VMEM((QUERY_HEADS, block, 1), jnp.float32),
            pltpu.VMEM((QUERY_HEADS, block, 1), jnp.float32),
            pltpu.VMEM((QUERY_HEADS, block, HEAD_SIZE), jnp.float32),
        ],
    )
    flops = 4 * steps * block * block * HEAD_SIZE * QUERY_HEADS
    return pl.pallas_call(
        lambda *refs: flash_kernel(*refs, block=block),
        grid_spec=grid_spec,
        out_shape=jax.ShapeDtypeStruct(query_rows.shape, jnp.bfloat16),
        compiler_params=pltpu.CompilerParams(dimension_semantics=("arbitrary",)),
        cost_estimate=pl.CostEstimate(
            flops=flops,
            transcendentals=steps * block * block * QUERY_HEADS,
            bytes_accessed=2 * query_rows.size * 2 + steps * block * kv_all.shape[-1] * 2,
        ),
        name="long_flash",
    )(info, query_rows, kv_all, kv_all)


def exchange_blocks(first, second):
    y_size = lax.axis_size("yl")
    x_size = lax.axis_size("xx")
    members = y_size * x_size
    firsts = [first]
    seconds = [second]
    for dy in range(y_size):
        for dx in range(x_size):
            if dy == 0 and dx == 0:
                continue
            moves = [
                (s, ((s // x_size + dy) % y_size) * x_size + (s % x_size + dx) % x_size)
                for s in range(members)
            ]
            firsts.append(lax.ppermute(first, ("yl", "xx"), moves))
            seconds.append(
                lax.ppermute(second, ("yl", "xx"), [(s, t) for s, t in moves if s > t])
            )
    pairs = [jnp.stack([a, b]) for a, b in zip(firsts, seconds)]
    return jnp.concatenate(pairs, axis=0)


def per_device(
    query_long,
    long_prompt_keys,
    long_prompt_values,
    long_length,
    short_prompt_queries,
    short_prompt_keys,
    short_prompt_values,
    short_prompt_index,
    page_owner,
    page_slot,
):
    half_rows = query_long.shape[1] // 2
    member = lax.axis_index("yl") * lax.axis_size("xx") + lax.axis_index("xx")
    group_id = lax.axis_index("r")
    length = lax.dynamic_index_in_dim(long_length[0], group_id, 0, keepdims=False)
    offsets = jnp.arange(half_rows, dtype=jnp.int32)
    pos_first = member * half_rows + offsets
    pos_second = (2 * SPAN - 1 - member) * half_rows + offsets

    key_row_block = long_prompt_keys[0]
    value_row_block = long_prompt_values[0]
    kv_rows = jnp.concatenate([key_row_block, value_row_block], axis=-1)

    kv_all = exchange_blocks(kv_rows[:half_rows], kv_rows[half_rows:])
    info = jnp.stack([member, length]).astype(jnp.int32)
    long_out = long_attention(info, query_long[0], kv_all, half_rows)

    segment_row = short_prompt_index[0, 0]
    order_ids = jnp.arange(segment_row.shape[0], dtype=jnp.int32)
    short_visible = (order_ids[None, :] <= order_ids[:, None]) & (
        segment_row[None, :] == segment_row[:, None]
    )
    short_stats = block_stats(
        short_prompt_queries[0][None],
        short_prompt_keys[0][None],
        short_prompt_values[0][None],
        short_visible[None],
    )
    short_prompt_output = finish_rows(take_pair(short_stats, 0), order_ids >= 0)

    row_positions = jnp.concatenate([pos_first, pos_second])
    kv_rows = jnp.where((row_positions < length)[:, None], kv_rows, jnp.zeros_like(kv_rows))
    page_count = kv_rows.shape[0] // PAGE
    page_width = kv_rows.shape[1]
    page_data = kv_rows.reshape(page_count, PAGE * page_width)
    owners = page_owner[0]
    slot_ids = page_slot[0]
    groups = lax.axis_size("grp")
    capacity = max(1, page_count // groups)
    page_ids = jnp.arange(page_count, dtype=jnp.int32)
    earlier = jnp.sum(
        (owners[None, :] == owners[:, None]) & (page_ids[None, :] < page_ids[:, None]), axis=1
    )
    target = owners * capacity + earlier
    bucket_ids = jnp.arange(groups * capacity, dtype=jnp.int32)
    onehot = target[None, :] == bucket_ids[:, None]
    outgoing = jnp.dot(
        onehot.astype(jnp.bfloat16), page_data, preferred_element_type=jnp.float32
    ).astype(jnp.bfloat16)
    out_slots = jnp.max(jnp.where(onehot, slot_ids[None, :], -1), axis=1)
    incoming, in_slots = (
        lax.all_to_all(
            outgoing.reshape(groups, capacity, PAGE * page_width),
            "grp",
            split_axis=0,
            concat_axis=0,
            tiled=True,
        ),
        lax.all_to_all(
            out_slots.reshape(groups, capacity), "grp", split_axis=0, concat_axis=0, tiled=True
        ),
    )
    chooser = in_slots.reshape(-1)[None, :] == page_ids[:, None]
    stored = jnp.dot(
        chooser.astype(jnp.bfloat16),
        incoming.reshape(groups * capacity, PAGE * page_width),
        preferred_element_type=jnp.float32,
    ).astype(jnp.bfloat16)
    return (
        long_out[None],
        short_prompt_output[None].astype(jnp.bfloat16),
        stored.reshape(1, page_count, PAGE, page_width),
    )


def solution(mesh):
    n_grp = mesh.shape["grp"]
    n_cp = mesh.shape["cp"]
    stride = n_cp // SPAN
    split_mesh = Mesh(
        mesh.devices.reshape(n_grp, 2, SPAN // 2, stride), ("grp", "yl", "xx", "r")
    )
    rows = ("yl", "xx", "r")
    in_specs = (
        P("grp", rows, None),
        P("grp", rows, None),
        P("grp", rows, None),
        P("grp", None),
        P("grp", rows, None),
        P("grp", rows, None),
        P("grp", rows, None),
        P("grp", rows, None),
        P("grp", rows),
        P("grp", rows),
    )
    out_specs = (P("grp", rows, None), P("grp", rows, None), P("grp", rows, None, None))
    return jax.shard_map(
        per_device, mesh=split_mesh, in_specs=in_specs, out_specs=out_specs, check_vma=False
    )
```

```python
import math

import jax
import jax.numpy as jnp
from jax import lax
from jax.experimental import pallas as pl
from jax.experimental.pallas import tpu as pltpu
from jax.sharding import Mesh
from jax.sharding import PartitionSpec as P

QUERY_HEADS = 8
KEY_VALUE_HEADS = 4
HEAD_SIZE = 128
PAGE = 128
SPAN = 8


def head_scores(query_rows, key_row_block, visible):
    paired_count, count_of_rows = (query_rows.shape[0], query_rows.shape[1])
    grouped_heads = query_rows.reshape(
        paired_count, count_of_rows, KEY_VALUE_HEADS, QUERY_HEADS // KEY_VALUE_HEADS, HEAD_SIZE
    )
    key_head_rows = key_row_block.reshape(
        paired_count, key_row_block.shape[1], KEY_VALUE_HEADS, HEAD_SIZE
    )
    scores = jnp.einsum(
        "prgjd,pkgd->pgjrk", grouped_heads, key_head_rows, preferred_element_type=jnp.float32
    )
    scores = scores / math.sqrt(HEAD_SIZE)
    return jnp.where(visible[:, None, None], scores, -jnp.inf)


def block_stats(query_rows, key_row_block, value_row_block, visible):
    scores = head_scores(query_rows, key_row_block, visible)
    highest = jnp.max(scores, axis=-1)
    anchor = jnp.where(jnp.isfinite(highest), highest, 0.0)
    weights = jnp.where(visible[:, None, None], jnp.exp(scores - anchor[..., None]), 0.0)
    weight_sum = jnp.sum(weights, axis=-1)
    value_head_rows = value_row_block.reshape(
        value_row_block.shape[0], value_row_block.shape[1], KEY_VALUE_HEADS, HEAD_SIZE
    )
    summed = jnp.einsum(
        "pgjrk,pkgd->pgjrd",
        weights.astype(jnp.bfloat16),
        value_head_rows,
        preferred_element_type=jnp.float32,
    )
    return (highest, weight_sum, summed)


def take_pair(pair_stats, position_in):
    return jax.tree.map(lambda leaf_array: leaf_array[position_in], pair_stats)


def finish_rows(stats_in, live_rows):
    highest, weight_sum, summed = stats_in
    divisor = jnp.where(weight_sum > 0, weight_sum, 1.0)
    result = summed / divisor[..., None]
    result = jnp.where(live_rows[None, None, :, None], result, 0.0)
    return jnp.transpose(result, (2, 0, 1, 3)).reshape(live_rows.shape[0], QUERY_HEADS * HEAD_SIZE)


def flash_kernel(info_ref, q_ref, k_ref, v_ref, o_ref, m_sc, l_sc, acc_sc, *, block):
    step = pl.program_id(0)
    member = info_ref[0]
    length = info_ref[1]
    later = step > member
    bq = jnp.where(later, 2 * SPAN - 1 - member, member)
    kc = jnp.where(later, step - member - 1, step)
    kmax = jnp.minimum(bq, (length - 1) // block)
    scale = 1.0 / math.sqrt(HEAD_SIZE)

    @pl.when(kc == 0)
    def _init():
        m_sc[...] = jnp.full(m_sc.shape, -jnp.inf, jnp.float32)
        l_sc[...] = jnp.zeros(l_sc.shape, jnp.float32)
        acc_sc[...] = jnp.zeros(acc_sc.shape, jnp.float32)

    per_group = QUERY_HEADS // KEY_VALUE_HEADS
    lane_tiles = block // HEAD_SIZE

    def attend(visible):
        for g in range(KEY_VALUE_HEADS):
            k = k_ref[0, :, g * HEAD_SIZE:(g + 1) * HEAD_SIZE]
            v = v_ref[0, :, g * HEAD_SIZE:(g + 1) * HEAD_SIZE]
            q = jnp.concatenate(
                [
                    q_ref[:, (g * per_group + jj) * HEAD_SIZE:(g * per_group + jj + 1) * HEAD_SIZE]
                    for jj in range(per_group)
                ],
                axis=0,
            )
            s = lax.dot_general(
                q, k, (((1,), (1,)), ((), ())), preferred_element_type=jnp.float32
            ) * scale
            if visible is not None:
                s = jnp.where(visible, s, -jnp.inf)
            m_old = m_sc[g]
            m_new = jnp.maximum(m_old, jnp.max(s, axis=-1, keepdims=True))
            if visible is not None:
                anchor = jnp.where(m_new > -jnp.inf, m_new, 0.0)
                p = jnp.where(visible, jnp.exp(s - jnp.concatenate([anchor] * lane_tiles, axis=1)), 0.0)
            else:
                anchor = m_new
                p = jnp.exp(s - jnp.concatenate([anchor] * lane_tiles, axis=1))
            alpha = jnp.exp(m_old - anchor)
            l_sc[g] = alpha * l_sc[g] + jnp.sum(p, axis=-1, keepdims=True)
            acc_sc[g] = alpha * acc_sc[g] + jnp.dot(
                p.astype(jnp.bfloat16), v, preferred_element_type=jnp.float32
            )
            m_sc[g] = m_new

    edge = (kc == bq) | ((kc + 1) * block > length)

    @pl.when((kc <= kmax) & edge)
    def _edge_step():
        q_pos = bq * block + lax.broadcasted_iota(jnp.int32, (block, block), 0)
        k_pos = kc * block + lax.broadcasted_iota(jnp.int32, (block, block), 1)
        visible = (k_pos <= q_pos) & (k_pos < length)
        attend(jnp.concatenate([visible] * per_group, axis=0))

    @pl.when((kc <= kmax) & jnp.logical_not(edge))
    def _full_step():
        attend(None)

    @pl.when(kc == bq)
    def _finish():
        live = (bq * block + lax.broadcasted_iota(jnp.int32, (block, 1), 0)) < length
        for g in range(KEY_VALUE_HEADS):
            l = l_sc[g]
            divisor = jnp.where(l > 0, l, 1.0)
            result = acc_sc[g] / divisor
            for jj in range(per_group):
                h = g * per_group + jj
                rows = result[jj * block:(jj + 1) * block]
                o_ref[:, h * HEAD_SIZE:(h + 1) * HEAD_SIZE] = jnp.where(live, rows, 0.0).astype(
                    o_ref.dtype
                )


def long_attention(info, query_rows, kv_all, block):
    steps = 2 * SPAN + 1
    half_kv = kv_all.shape[-1] // 2
    x_size = SPAN // 2

    def q_index(step, info_ref):
        return (jnp.where(step > info_ref[0], 1, 0), 0)

    def kv_index(step, info_ref, which):
        member = info_ref[0]
        length = info_ref[1]
        later = step > member
        bq = jnp.where(later, 2 * SPAN - 1 - member, member)
        kc = jnp.where(later, step - member - 1, step)
        kk = jnp.minimum(kc, jnp.minimum(bq, (length - 1) // block))
        source = jnp.where(kk < SPAN, kk, 2 * SPAN - 1 - kk)
        half = jnp.where(kk < SPAN, 0, 1)
        j = (source % x_size) * 4 + (source // x_size) * 2 + half
        return (j, 0, which)

    grid_spec = pltpu.PrefetchScalarGridSpec(
        num_scalar_prefetch=1,
        grid=(steps,),
        in_specs=[
            pl.BlockSpec((block, query_rows.shape[1]), q_index),
            pl.BlockSpec((1, block, half_kv), lambda step, info_ref: kv_index(step, info_ref, 0)),
            pl.BlockSpec((1, block, half_kv), lambda step, info_ref: kv_index(step, info_ref, 1)),
        ],
        out_specs=pl.BlockSpec((block, query_rows.shape[1]), q_index),
        scratch_shapes=[
            pltpu.VMEM((KEY_VALUE_HEADS, QUERY_HEADS // KEY_VALUE_HEADS * block, HEAD_SIZE), jnp.float32),
            pltpu.VMEM((KEY_VALUE_HEADS, QUERY_HEADS // KEY_VALUE_HEADS * block, HEAD_SIZE), jnp.float32),
            pltpu.VMEM((KEY_VALUE_HEADS, QUERY_HEADS // KEY_VALUE_HEADS * block, HEAD_SIZE), jnp.float32),
        ],
    )
    flops = 4 * steps * block * block * HEAD_SIZE * QUERY_HEADS
    return pl.pallas_call(
        lambda *refs: flash_kernel(*refs, block=block),
        grid_spec=grid_spec,
        out_shape=jax.ShapeDtypeStruct(query_rows.shape, jnp.bfloat16),
        compiler_params=pltpu.CompilerParams(dimension_semantics=("arbitrary",)),
        cost_estimate=pl.CostEstimate(
            flops=flops,
            transcendentals=steps * block * block * QUERY_HEADS,
            bytes_accessed=2 * query_rows.size * 2 + steps * block * kv_all.shape[-1] * 2,
        ),
        name="long_flash",
    )(info, query_rows, kv_all, kv_all)


def per_device(
    query_long,
    long_prompt_keys,
    long_prompt_values,
    long_length,
    short_prompt_queries,
    short_prompt_keys,
    short_prompt_values,
    short_prompt_index,
    page_owner,
    page_slot,
):
    half_rows = query_long.shape[1] // 2
    member = lax.axis_index("yl") * lax.axis_size("xx") + lax.axis_index("xx")
    group_id = lax.axis_index("r")
    length = lax.dynamic_index_in_dim(long_length[0], group_id, 0, keepdims=False)
    offsets = jnp.arange(half_rows, dtype=jnp.int32)
    pos_first = member * half_rows + offsets
    pos_second = (2 * SPAN - 1 - member) * half_rows + offsets

    key_row_block = long_prompt_keys[0]
    value_row_block = long_prompt_values[0]
    kv_rows = jnp.concatenate([key_row_block, value_row_block], axis=-1)

    kv_pair = lax.all_gather(kv_rows, "yl", axis=0, tiled=False)
    kv_all = lax.all_gather(kv_pair, "xx", axis=0, tiled=False)
    kv_all = kv_all.reshape(2 * SPAN, half_rows, kv_rows.shape[-1])
    info = jnp.stack([member, length]).astype(jnp.int32)
    long_out = long_attention(info, query_long[0], kv_all, half_rows)

    segment_row = short_prompt_index[0, 0]
    order_ids = jnp.arange(segment_row.shape[0], dtype=jnp.int32)
    short_visible = (order_ids[None, :] <= order_ids[:, None]) & (
        segment_row[None, :] == segment_row[:, None]
    )
    short_stats = block_stats(
        short_prompt_queries[0][None],
        short_prompt_keys[0][None],
        short_prompt_values[0][None],
        short_visible[None],
    )
    short_prompt_output = finish_rows(take_pair(short_stats, 0), order_ids >= 0)

    row_positions = jnp.concatenate([pos_first, pos_second])
    kv_rows = jnp.where((row_positions < length)[:, None], kv_rows, jnp.zeros_like(kv_rows))
    page_count = kv_rows.shape[0] // PAGE
    page_width = kv_rows.shape[1]
    page_data = kv_rows.reshape(page_count, PAGE * page_width)
    owners = page_owner[0]
    slot_ids = page_slot[0]
    groups = lax.axis_size("grp")
    capacity = max(1, page_count // groups)
    page_ids = jnp.arange(page_count, dtype=jnp.int32)
    earlier = jnp.sum(
        (owners[None, :] == owners[:, None]) & (page_ids[None, :] < page_ids[:, None]), axis=1
    )
    target = owners * capacity + earlier
    bucket_ids = jnp.arange(groups * capacity, dtype=jnp.int32)
    onehot = target[None, :] == bucket_ids[:, None]
    outgoing = jnp.dot(
        onehot.astype(jnp.bfloat16), page_data, preferred_element_type=jnp.float32
    ).astype(jnp.bfloat16)
    out_slots = jnp.max(jnp.where(onehot, slot_ids[None, :], -1), axis=1)
    incoming, in_slots = (
        lax.all_to_all(
            outgoing.reshape(groups, capacity, PAGE * page_width),
            "grp",
            split_axis=0,
            concat_axis=0,
            tiled=True,
        ),
        lax.all_to_all(
            out_slots.reshape(groups, capacity), "grp", split_axis=0, concat_axis=0, tiled=True
        ),
    )
    chooser = in_slots.reshape(-1)[None, :] == page_ids[:, None]
    stored = jnp.dot(
        chooser.astype(jnp.bfloat16),
        incoming.reshape(groups * capacity, PAGE * page_width),
        preferred_element_type=jnp.float32,
    ).astype(jnp.bfloat16)
    return (
        long_out[None],
        short_prompt_output[None].astype(jnp.bfloat16),
        stored.reshape(1, page_count, PAGE, page_width),
    )


def solution(mesh):
    n_grp = mesh.shape["grp"]
    n_cp = mesh.shape["cp"]
    stride = n_cp // SPAN
    split_mesh = Mesh(
        mesh.devices.reshape(n_grp, 2, SPAN // 2, stride), ("grp", "yl", "xx", "r")
    )
    rows = ("yl", "xx", "r")
    in_specs = (
        P("grp", rows, None),
        P("grp", rows, None),
        P("grp", rows, None),
        P("grp", None),
        P("grp", rows, None),
        P("grp", rows, None),
        P("grp", rows, None),
        P("grp", rows, None),
        P("grp", rows),
        P("grp", rows),
    )
    out_specs = (P("grp", rows, None), P("grp", rows, None), P("grp", rows, None, None))
    return jax.shard_map(
        per_device, mesh=split_mesh, in_specs=in_specs, out_specs=out_specs, check_vma=False
    )
```

```python
import math

import jax
import jax.numpy as jnp
from jax import lax
from jax.experimental import pallas as pl
from jax.experimental.pallas import tpu as pltpu
from jax.sharding import Mesh
from jax.sharding import PartitionSpec as P

QUERY_HEADS = 8
KEY_VALUE_HEADS = 4
HEAD_SIZE = 128
PAGE = 128
SPAN = 8


def head_scores(query_rows, key_row_block, visible):
    paired_count, count_of_rows = (query_rows.shape[0], query_rows.shape[1])
    grouped_heads = query_rows.reshape(
        paired_count, count_of_rows, KEY_VALUE_HEADS, QUERY_HEADS // KEY_VALUE_HEADS, HEAD_SIZE
    )
    key_head_rows = key_row_block.reshape(
        paired_count, key_row_block.shape[1], KEY_VALUE_HEADS, HEAD_SIZE
    )
    scores = jnp.einsum(
        "prgjd,pkgd->pgjrk", grouped_heads, key_head_rows, preferred_element_type=jnp.float32
    )
    scores = scores / math.sqrt(HEAD_SIZE)
    return jnp.where(visible[:, None, None], scores, -jnp.inf)


def block_stats(query_rows, key_row_block, value_row_block, visible):
    scores = head_scores(query_rows, key_row_block, visible)
    highest = jnp.max(scores, axis=-1)
    anchor = jnp.where(jnp.isfinite(highest), highest, 0.0)
    weights = jnp.where(visible[:, None, None], jnp.exp(scores - anchor[..., None]), 0.0)
    weight_sum = jnp.sum(weights, axis=-1)
    value_head_rows = value_row_block.reshape(
        value_row_block.shape[0], value_row_block.shape[1], KEY_VALUE_HEADS, HEAD_SIZE
    )
    summed = jnp.einsum(
        "pgjrk,pkgd->pgjrd",
        weights.astype(jnp.bfloat16),
        value_head_rows,
        preferred_element_type=jnp.float32,
    )
    return (highest, weight_sum, summed)


def take_pair(pair_stats, position_in):
    return jax.tree.map(lambda leaf_array: leaf_array[position_in], pair_stats)


def finish_rows(stats_in, live_rows):
    highest, weight_sum, summed = stats_in
    divisor = jnp.where(weight_sum > 0, weight_sum, 1.0)
    result = summed / divisor[..., None]
    result = jnp.where(live_rows[None, None, :, None], result, 0.0)
    return jnp.transpose(result, (2, 0, 1, 3)).reshape(live_rows.shape[0], QUERY_HEADS * HEAD_SIZE)


def flash_kernel(info_ref, q_ref, k_ref, v_ref, o_ref, m_sc, l_sc, acc_sc, *, block):
    step = pl.program_id(0)
    member = info_ref[0]
    length = info_ref[1]
    later = step > member
    bq = jnp.where(later, 2 * SPAN - 1 - member, member)
    kc = jnp.where(later, step - member - 1, step)
    kmax = jnp.minimum(bq, (length - 1) // block)
    scale = 1.0 / math.sqrt(HEAD_SIZE)

    @pl.when(kc == 0)
    def _init():
        m_sc[...] = jnp.full(m_sc.shape, -jnp.inf, jnp.float32)
        l_sc[...] = jnp.zeros(l_sc.shape, jnp.float32)
        acc_sc[...] = jnp.zeros(acc_sc.shape, jnp.float32)

    per_group = QUERY_HEADS // KEY_VALUE_HEADS
    lane_tiles = block // HEAD_SIZE

    def attend(visible):
        for g in range(KEY_VALUE_HEADS):
            k = k_ref[0, :, g * HEAD_SIZE:(g + 1) * HEAD_SIZE]
            v = v_ref[0, :, g * HEAD_SIZE:(g + 1) * HEAD_SIZE]
            q = jnp.concatenate(
                [
                    q_ref[:, (g * per_group + jj) * HEAD_SIZE:(g * per_group + jj + 1) * HEAD_SIZE]
                    for jj in range(per_group)
                ],
                axis=0,
            )
            s = lax.dot_general(
                q, k, (((1,), (1,)), ((), ())), preferred_element_type=jnp.float32
            ) * scale
            if visible is not None:
                s = jnp.where(visible, s, -jnp.inf)
            m_old = m_sc[g]
            m_new = jnp.maximum(m_old, jnp.max(s, axis=-1, keepdims=True))
            if visible is not None:
                anchor = jnp.where(m_new > -jnp.inf, m_new, 0.0)
                p = jnp.where(visible, jnp.exp(s - jnp.concatenate([anchor] * lane_tiles, axis=1)), 0.0)
            else:
                anchor = m_new
                p = jnp.exp(s - jnp.concatenate([anchor] * lane_tiles, axis=1))
            alpha = jnp.exp(m_old - anchor)
            l_sc[g] = alpha * l_sc[g] + jnp.sum(p, axis=-1, keepdims=True)
            acc_sc[g] = alpha * acc_sc[g] + jnp.dot(
                p.astype(jnp.bfloat16), v, preferred_element_type=jnp.float32
            )
            m_sc[g] = m_new

    edge = (kc == bq) | ((kc + 1) * block > length)

    @pl.when((kc <= kmax) & edge)
    def _edge_step():
        q_pos = bq * block + lax.broadcasted_iota(jnp.int32, (block, block), 0)
        k_pos = kc * block + lax.broadcasted_iota(jnp.int32, (block, block), 1)
        visible = (k_pos <= q_pos) & (k_pos < length)
        attend(jnp.concatenate([visible] * per_group, axis=0))

    @pl.when((kc <= kmax) & jnp.logical_not(edge))
    def _full_step():
        attend(None)

    @pl.when(kc == bq)
    def _finish():
        live = (bq * block + lax.broadcasted_iota(jnp.int32, (block, 1), 0)) < length
        for g in range(KEY_VALUE_HEADS):
            l = l_sc[g]
            divisor = jnp.where(l > 0, l, 1.0)
            result = acc_sc[g] / divisor
            for jj in range(per_group):
                h = g * per_group + jj
                rows = result[jj * block:(jj + 1) * block]
                o_ref[:, h * HEAD_SIZE:(h + 1) * HEAD_SIZE] = jnp.where(live, rows, 0.0).astype(
                    o_ref.dtype
                )


def long_attention(info, query_rows, kv_all, block):
    steps = 2 * SPAN + 1
    half_kv = kv_all.shape[-1] // 2
    x_size = SPAN // 2

    def q_index(step, info_ref):
        return (jnp.where(step > info_ref[0], 1, 0), 0)

    def kv_index(step, info_ref, which):
        member = info_ref[0]
        length = info_ref[1]
        later = step > member
        bq = jnp.where(later, 2 * SPAN - 1 - member, member)
        kc = jnp.where(later, step - member - 1, step)
        kk = jnp.minimum(kc, jnp.minimum(bq, (length - 1) // block))
        source = jnp.where(kk < SPAN, kk, 2 * SPAN - 1 - kk)
        half = jnp.where(kk < SPAN, 0, 1)
        other_row = jnp.where(source // x_size == member // x_size, 0, 1)
        j = (source % x_size) * 4 + other_row * 2 + half
        return (j, 0, which)

    grid_spec = pltpu.PrefetchScalarGridSpec(
        num_scalar_prefetch=1,
        grid=(steps,),
        in_specs=[
            pl.BlockSpec((block, query_rows.shape[1]), q_index),
            pl.BlockSpec((1, block, half_kv), lambda step, info_ref: kv_index(step, info_ref, 0)),
            pl.BlockSpec((1, block, half_kv), lambda step, info_ref: kv_index(step, info_ref, 1)),
        ],
        out_specs=pl.BlockSpec((block, query_rows.shape[1]), q_index),
        scratch_shapes=[
            pltpu.VMEM((KEY_VALUE_HEADS, QUERY_HEADS // KEY_VALUE_HEADS * block, HEAD_SIZE), jnp.float32),
            pltpu.VMEM((KEY_VALUE_HEADS, QUERY_HEADS // KEY_VALUE_HEADS * block, HEAD_SIZE), jnp.float32),
            pltpu.VMEM((KEY_VALUE_HEADS, QUERY_HEADS // KEY_VALUE_HEADS * block, HEAD_SIZE), jnp.float32),
        ],
    )
    flops = 4 * steps * block * block * HEAD_SIZE * QUERY_HEADS
    return pl.pallas_call(
        lambda *refs: flash_kernel(*refs, block=block),
        grid_spec=grid_spec,
        out_shape=jax.ShapeDtypeStruct(query_rows.shape, jnp.bfloat16),
        compiler_params=pltpu.CompilerParams(dimension_semantics=("arbitrary",)),
        cost_estimate=pl.CostEstimate(
            flops=flops,
            transcendentals=steps * block * block * QUERY_HEADS,
            bytes_accessed=2 * query_rows.size * 2 + steps * block * kv_all.shape[-1] * 2,
        ),
        name="long_flash",
    )(info, query_rows, kv_all, kv_all)


def per_device(
    query_long,
    long_prompt_keys,
    long_prompt_values,
    long_length,
    short_prompt_queries,
    short_prompt_keys,
    short_prompt_values,
    short_prompt_index,
    page_owner,
    page_slot,
):
    half_rows = query_long.shape[1] // 2
    member = lax.axis_index("yl") * lax.axis_size("xx") + lax.axis_index("xx")
    group_id = lax.axis_index("r")
    length = lax.dynamic_index_in_dim(long_length[0], group_id, 0, keepdims=False)
    offsets = jnp.arange(half_rows, dtype=jnp.int32)
    pos_first = member * half_rows + offsets
    pos_second = (2 * SPAN - 1 - member) * half_rows + offsets

    key_row_block = long_prompt_keys[0]
    value_row_block = long_prompt_values[0]
    kv_rows = jnp.concatenate([key_row_block, value_row_block], axis=-1)

    y_size = lax.axis_size("yl")
    partner = lax.ppermute(kv_rows, "yl", [(i, (i + 1) % y_size) for i in range(y_size)])
    kv_pair = jnp.stack([kv_rows, partner])
    kv_all = lax.all_gather(kv_pair, "xx", axis=0, tiled=False)
    kv_all = kv_all.reshape(2 * SPAN, half_rows, kv_rows.shape[-1])
    info = jnp.stack([member, length]).astype(jnp.int32)
    long_out = long_attention(info, query_long[0], kv_all, half_rows)

    segment_row = short_prompt_index[0, 0]
    order_ids = jnp.arange(segment_row.shape[0], dtype=jnp.int32)
    short_visible = (order_ids[None, :] <= order_ids[:, None]) & (
        segment_row[None, :] == segment_row[:, None]
    )
    short_stats = block_stats(
        short_prompt_queries[0][None],
        short_prompt_keys[0][None],
        short_prompt_values[0][None],
        short_visible[None],
    )
    short_prompt_output = finish_rows(take_pair(short_stats, 0), order_ids >= 0)

    row_positions = jnp.concatenate([pos_first, pos_second])
    kv_rows = jnp.where((row_positions < length)[:, None], kv_rows, jnp.zeros_like(kv_rows))
    page_count = kv_rows.shape[0] // PAGE
    page_width = kv_rows.shape[1]
    page_data = kv_rows.reshape(page_count, PAGE * page_width)
    owners = page_owner[0]
    slot_ids = page_slot[0]
    groups = lax.axis_size("grp")
    capacity = max(1, page_count // groups)
    page_ids = jnp.arange(page_count, dtype=jnp.int32)
    earlier = jnp.sum(
        (owners[None, :] == owners[:, None]) & (page_ids[None, :] < page_ids[:, None]), axis=1
    )
    target = owners * capacity + earlier
    bucket_ids = jnp.arange(groups * capacity, dtype=jnp.int32)
    onehot = target[None, :] == bucket_ids[:, None]
    outgoing = jnp.dot(
        onehot.astype(jnp.bfloat16), page_data, preferred_element_type=jnp.float32
    ).astype(jnp.bfloat16)
    out_slots = jnp.max(jnp.where(onehot, slot_ids[None, :], -1), axis=1)
    incoming, in_slots = (
        lax.all_to_all(
            outgoing.reshape(groups, capacity, PAGE * page_width),
            "grp",
            split_axis=0,
            concat_axis=0,
            tiled=True,
        ),
        lax.all_to_all(
            out_slots.reshape(groups, capacity), "grp", split_axis=0, concat_axis=0, tiled=True
        ),
    )
    chooser = in_slots.reshape(-1)[None, :] == page_ids[:, None]
    stored = jnp.dot(
        chooser.astype(jnp.bfloat16),
        incoming.reshape(groups * capacity, PAGE * page_width),
        preferred_element_type=jnp.float32,
    ).astype(jnp.bfloat16)
    return (
        long_out[None],
        short_prompt_output[None].astype(jnp.bfloat16),
        stored.reshape(1, page_count, PAGE, page_width),
    )


def solution(mesh):
    n_grp = mesh.shape["grp"]
    n_cp = mesh.shape["cp"]
    stride = n_cp // SPAN
    split_mesh = Mesh(
        mesh.devices.reshape(n_grp, 2, SPAN // 2, stride), ("grp", "yl", "xx", "r")
    )
    rows = ("yl", "xx", "r")
    in_specs = (
        P("grp", rows, None),
        P("grp", rows, None),
        P("grp", rows, None),
        P("grp", None),
        P("grp", rows, None),
        P("grp", rows, None),
        P("grp", rows, None),
        P("grp", rows, None),
        P("grp", rows),
        P("grp", rows),
    )
    out_specs = (P("grp", rows, None), P("grp", rows, None), P("grp", rows, None, None))
    return jax.shard_map(
        per_device, mesh=split_mesh, in_specs=in_specs, out_specs=out_specs, check_vma=False
    )
```

```python
import math

import jax
import jax.numpy as jnp
from jax import lax
from jax.experimental import pallas as pl
from jax.experimental.pallas import tpu as pltpu
from jax.sharding import Mesh
from jax.sharding import PartitionSpec as P

QUERY_HEADS = 8
KEY_VALUE_HEADS = 4
HEAD_SIZE = 128
PAGE = 128
SPAN = 8


def head_scores(query_rows, key_row_block, visible):
    paired_count, count_of_rows = (query_rows.shape[0], query_rows.shape[1])
    grouped_heads = query_rows.reshape(
        paired_count, count_of_rows, KEY_VALUE_HEADS, QUERY_HEADS // KEY_VALUE_HEADS, HEAD_SIZE
    )
    key_head_rows = key_row_block.reshape(
        paired_count, key_row_block.shape[1], KEY_VALUE_HEADS, HEAD_SIZE
    )
    scores = jnp.einsum(
        "prgjd,pkgd->pgjrk", grouped_heads, key_head_rows, preferred_element_type=jnp.float32
    )
    scores = scores / math.sqrt(HEAD_SIZE)
    return jnp.where(visible[:, None, None], scores, -jnp.inf)


def block_stats(query_rows, key_row_block, value_row_block, visible):
    scores = head_scores(query_rows, key_row_block, visible)
    highest = jnp.max(scores, axis=-1)
    anchor = jnp.where(jnp.isfinite(highest), highest, 0.0)
    weights = jnp.where(visible[:, None, None], jnp.exp(scores - anchor[..., None]), 0.0)
    weight_sum = jnp.sum(weights, axis=-1)
    value_head_rows = value_row_block.reshape(
        value_row_block.shape[0], value_row_block.shape[1], KEY_VALUE_HEADS, HEAD_SIZE
    )
    summed = jnp.einsum(
        "pgjrk,pkgd->pgjrd",
        weights.astype(jnp.bfloat16),
        value_head_rows,
        preferred_element_type=jnp.float32,
    )
    return (highest, weight_sum, summed)


def take_pair(pair_stats, position_in):
    return jax.tree.map(lambda leaf_array: leaf_array[position_in], pair_stats)


def finish_rows(stats_in, live_rows):
    highest, weight_sum, summed = stats_in
    divisor = jnp.where(weight_sum > 0, weight_sum, 1.0)
    result = summed / divisor[..., None]
    result = jnp.where(live_rows[None, None, :, None], result, 0.0)
    return jnp.transpose(result, (2, 0, 1, 3)).reshape(live_rows.shape[0], QUERY_HEADS * HEAD_SIZE)


def flash_kernel(info_ref, q_ref, k_ref, v_ref, o_ref, m_sc, l_sc, acc_sc, *, block):
    step = pl.program_id(0)
    member = info_ref[0]
    length = info_ref[1]
    later = step > member
    bq = jnp.where(later, 2 * SPAN - 1 - member, member)
    kc = jnp.where(later, step - member - 1, step)
    kmax = jnp.minimum(bq, (length - 1) // block)
    scale = 1.0 / math.sqrt(HEAD_SIZE)

    @pl.when(kc == 0)
    def _init():
        m_sc[...] = jnp.full(m_sc.shape, -jnp.inf, jnp.float32)
        l_sc[...] = jnp.zeros(l_sc.shape, jnp.float32)
        acc_sc[...] = jnp.zeros(acc_sc.shape, jnp.float32)

    per_group = QUERY_HEADS // KEY_VALUE_HEADS
    lane_tiles = block // HEAD_SIZE

    def attend(visible):
        for g in range(KEY_VALUE_HEADS):
            k = k_ref[0, :, g * HEAD_SIZE:(g + 1) * HEAD_SIZE]
            v = v_ref[0, :, g * HEAD_SIZE:(g + 1) * HEAD_SIZE]
            q = jnp.concatenate(
                [
                    q_ref[:, (g * per_group + jj) * HEAD_SIZE:(g * per_group + jj + 1) * HEAD_SIZE]
                    for jj in range(per_group)
                ],
                axis=0,
            )
            s = lax.dot_general(
                q, k, (((1,), (1,)), ((), ())), preferred_element_type=jnp.float32
            ) * scale
            if visible is not None:
                s = jnp.where(visible, s, -jnp.inf)
            m_old = m_sc[g]
            m_new = jnp.maximum(m_old, jnp.max(s, axis=-1, keepdims=True))
            if visible is not None:
                anchor = jnp.where(m_new > -jnp.inf, m_new, 0.0)
                p = jnp.where(visible, jnp.exp(s - jnp.concatenate([anchor] * lane_tiles, axis=1)), 0.0)
            else:
                anchor = m_new
                p = jnp.exp(s - jnp.concatenate([anchor] * lane_tiles, axis=1))
            alpha = jnp.exp(m_old - anchor)
            l_sc[g] = alpha * l_sc[g] + jnp.sum(p, axis=-1, keepdims=True)
            acc_sc[g] = alpha * acc_sc[g] + jnp.dot(
                p.astype(jnp.bfloat16), v, preferred_element_type=jnp.float32
            )
            m_sc[g] = m_new

    edge = (kc == bq) | ((kc + 1) * block > length)

    @pl.when((kc <= kmax) & edge)
    def _edge_step():
        q_pos = bq * block + lax.broadcasted_iota(jnp.int32, (block, block), 0)
        k_pos = kc * block + lax.broadcasted_iota(jnp.int32, (block, block), 1)
        visible = (k_pos <= q_pos) & (k_pos < length)
        attend(jnp.concatenate([visible] * per_group, axis=0))

    @pl.when((kc <= kmax) & jnp.logical_not(edge))
    def _full_step():
        attend(None)

    @pl.when(kc == bq)
    def _finish():
        live = (bq * block + lax.broadcasted_iota(jnp.int32, (block, 1), 0)) < length
        for g in range(KEY_VALUE_HEADS):
            l = l_sc[g]
            divisor = jnp.where(l > 0, l, 1.0)
            result = acc_sc[g] / divisor
            for jj in range(per_group):
                h = g * per_group + jj
                rows = result[jj * block:(jj + 1) * block]
                o_ref[:, h * HEAD_SIZE:(h + 1) * HEAD_SIZE] = jnp.where(live, rows, 0.0).astype(
                    o_ref.dtype
                )


def long_attention(info, query_rows, kv_all, block):
    steps = 2 * SPAN + 1
    half_kv = kv_all.shape[-1] // 2
    x_size = SPAN // 2

    def q_index(step, info_ref):
        return (jnp.where(step > info_ref[0], 1, 0), 0)

    def kv_index(step, info_ref, which):
        member = info_ref[0]
        length = info_ref[1]
        later = step > member
        bq = jnp.where(later, 2 * SPAN - 1 - member, member)
        kc = jnp.where(later, step - member - 1, step)
        kk = jnp.minimum(kc, jnp.minimum(bq, (length - 1) // block))
        source = jnp.where(kk < SPAN, kk, 2 * SPAN - 1 - kk)
        half = jnp.where(kk < SPAN, 0, 1)
        other_row = jnp.where(source // x_size == member // x_size, 0, 1)
        j = (source % x_size) * 4 + other_row * 2 + half
        return (j, 0, which)

    grid_spec = pltpu.PrefetchScalarGridSpec(
        num_scalar_prefetch=1,
        grid=(steps,),
        in_specs=[
            pl.BlockSpec((block, query_rows.shape[1]), q_index),
            pl.BlockSpec((1, block, half_kv), lambda step, info_ref: kv_index(step, info_ref, 0)),
            pl.BlockSpec((1, block, half_kv), lambda step, info_ref: kv_index(step, info_ref, 1)),
        ],
        out_specs=pl.BlockSpec((block, query_rows.shape[1]), q_index),
        scratch_shapes=[
            pltpu.VMEM((KEY_VALUE_HEADS, QUERY_HEADS // KEY_VALUE_HEADS * block, HEAD_SIZE), jnp.float32),
            pltpu.VMEM((KEY_VALUE_HEADS, QUERY_HEADS // KEY_VALUE_HEADS * block, HEAD_SIZE), jnp.float32),
            pltpu.VMEM((KEY_VALUE_HEADS, QUERY_HEADS // KEY_VALUE_HEADS * block, HEAD_SIZE), jnp.float32),
        ],
    )
    flops = 4 * steps * block * block * HEAD_SIZE * QUERY_HEADS
    return pl.pallas_call(
        lambda *refs: flash_kernel(*refs, block=block),
        grid_spec=grid_spec,
        out_shape=jax.ShapeDtypeStruct(query_rows.shape, jnp.bfloat16),
        compiler_params=pltpu.CompilerParams(dimension_semantics=("arbitrary",)),
        cost_estimate=pl.CostEstimate(
            flops=flops,
            transcendentals=steps * block * block * QUERY_HEADS,
            bytes_accessed=2 * query_rows.size * 2 + steps * block * kv_all.shape[-1] * 2,
        ),
        name="long_flash",
    )(info, query_rows, kv_all, kv_all)


def per_device(
    query_long,
    long_prompt_keys,
    long_prompt_values,
    long_length,
    short_prompt_queries,
    short_prompt_keys,
    short_prompt_values,
    short_prompt_index,
    page_owner,
    page_slot,
):
    half_rows = query_long.shape[1] // 2
    member = lax.axis_index("yl") * lax.axis_size("xx") + lax.axis_index("xx")
    group_id = lax.axis_index("r")
    length = lax.dynamic_index_in_dim(long_length[0], group_id, 0, keepdims=False)
    offsets = jnp.arange(half_rows, dtype=jnp.int32)
    pos_first = member * half_rows + offsets
    pos_second = (2 * SPAN - 1 - member) * half_rows + offsets

    key_row_block = long_prompt_keys[0]
    value_row_block = long_prompt_values[0]
    kv_rows = jnp.concatenate([key_row_block, value_row_block], axis=-1)

    y_size = lax.axis_size("yl")
    partner = lax.ppermute(kv_rows, "yl", [(i, (i + 1) % y_size) for i in range(y_size)])
    kv_own_row = lax.all_gather(kv_rows, "xx", axis=0, tiled=False)
    kv_other_row = lax.all_gather(partner, "xx", axis=0, tiled=False)
    kv_all = jnp.stack([kv_own_row, kv_other_row], axis=1)
    kv_all = kv_all.reshape(2 * SPAN, half_rows, kv_rows.shape[-1])
    info = jnp.stack([member, length]).astype(jnp.int32)
    long_out = long_attention(info, query_long[0], kv_all, half_rows)

    segment_row = short_prompt_index[0, 0]
    order_ids = jnp.arange(segment_row.shape[0], dtype=jnp.int32)
    short_visible = (order_ids[None, :] <= order_ids[:, None]) & (
        segment_row[None, :] == segment_row[:, None]
    )
    short_stats = block_stats(
        short_prompt_queries[0][None],
        short_prompt_keys[0][None],
        short_prompt_values[0][None],
        short_visible[None],
    )
    short_prompt_output = finish_rows(take_pair(short_stats, 0), order_ids >= 0)

    row_positions = jnp.concatenate([pos_first, pos_second])
    kv_rows = jnp.where((row_positions < length)[:, None], kv_rows, jnp.zeros_like(kv_rows))
    page_count = kv_rows.shape[0] // PAGE
    page_width = kv_rows.shape[1]
    page_data = kv_rows.reshape(page_count, PAGE * page_width)
    owners = page_owner[0]
    slot_ids = page_slot[0]
    groups = lax.axis_size("grp")
    capacity = max(1, page_count // groups)
    page_ids = jnp.arange(page_count, dtype=jnp.int32)
    earlier = jnp.sum(
        (owners[None, :] == owners[:, None]) & (page_ids[None, :] < page_ids[:, None]), axis=1
    )
    target = owners * capacity + earlier
    bucket_ids = jnp.arange(groups * capacity, dtype=jnp.int32)
    onehot = target[None, :] == bucket_ids[:, None]
    outgoing = jnp.dot(
        onehot.astype(jnp.bfloat16), page_data, preferred_element_type=jnp.float32
    ).astype(jnp.bfloat16)
    out_slots = jnp.max(jnp.where(onehot, slot_ids[None, :], -1), axis=1)
    incoming, in_slots = (
        lax.all_to_all(
            outgoing.reshape(groups, capacity, PAGE * page_width),
            "grp",
            split_axis=0,
            concat_axis=0,
            tiled=True,
        ),
        lax.all_to_all(
            out_slots.reshape(groups, capacity), "grp", split_axis=0, concat_axis=0, tiled=True
        ),
    )
    chooser = in_slots.reshape(-1)[None, :] == page_ids[:, None]
    stored = jnp.dot(
        chooser.astype(jnp.bfloat16),
        incoming.reshape(groups * capacity, PAGE * page_width),
        preferred_element_type=jnp.float32,
    ).astype(jnp.bfloat16)
    return (
        long_out[None],
        short_prompt_output[None].astype(jnp.bfloat16),
        stored.reshape(1, page_count, PAGE, page_width),
    )


def solution(mesh):
    n_grp = mesh.shape["grp"]
    n_cp = mesh.shape["cp"]
    stride = n_cp // SPAN
    split_mesh = Mesh(
        mesh.devices.reshape(n_grp, 2, SPAN // 2, stride), ("grp", "yl", "xx", "r")
    )
    rows = ("yl", "xx", "r")
    in_specs = (
        P("grp", rows, None),
        P("grp", rows, None),
        P("grp", rows, None),
        P("grp", None),
        P("grp", rows, None),
        P("grp", rows, None),
        P("grp", rows, None),
        P("grp", rows, None),
        P("grp", rows),
        P("grp", rows),
    )
    out_specs = (P("grp", rows, None), P("grp", rows, None), P("grp", rows, None, None))
    return jax.shard_map(
        per_device, mesh=split_mesh, in_specs=in_specs, out_specs=out_specs, check_vma=False
    )
```
